32 devices in a mesh: replica: 4 (over y, core), fsdp: 2 (over x), tensor: 4 (over z).
Axes of the slice: x: 2, y: 2, z: 4, core: 2. Of those that a mesh axis runs over, the one named last changes fastest.
Arguments:
- grad_parts: bfloat16 [4, 2, 512, 8192], P('replica', 'fsdp', 'tensor'), may hold values from -12 to 12
- inner_params: float32 [4, 512, 8192], P('replica', 'tensor', 'fsdp'), may hold values from -0.12 to 0.12
- first_moment: float32 [4, 512, 8192], P('replica', 'tensor', 'fsdp'), may hold values from -4 to 4
- second_moment: float32 [4, 512, 8192], P('replica', 'tensor', 'fsdp'), may hold values from 0.1 to 10
- outer_params: float32 [4, 512, 2048], P('replica', 'tensor', 'fsdp'), may hold values from -0.12 to 0.12
- outer_momentum: float32 [4, 512, 2048], P('replica', 'tensor', 'fsdp'), may hold values from -0.06 to 0.06
Outputs:
- next_weights: float32 [512, 8192], P('tensor')
- outer_params_out: float32 [4, 512, 2048], P('replica', 'tensor', 'fsdp')
- outer_momentum_out: float32 [4, 512, 2048], P('replica', 'tensor', 'fsdp')
- first_out: float32 [4, 512, 8192], P('replica', 'tensor', 'fsdp')
- second_out: float32 [4, 512, 8192], P('replica', 'tensor', 'fsdp')
The draws below stay inside these ranges and needn't reach their ends.
All inputs are finite; a program needn't handle non-finite values.
Results may differ from the reference program's by a relative error of at most 0.0003.
Values may be sent and summed in bfloat16 or wider, within the bound.
No kernel may reach another device: no remote copies, remote signals or barrier semaphores. Data moves between devices by JAX's collectives and lax.ppermute only.
A program may use at most 64 MiB of HBM per device.

```python
import math
import jax
import jax.numpy as jnp
from jax import lax

D = 8192
STEP = 100
KVW = 512
REPLICAS = 4
SHARE = 1024
OUTER_COLS = 2048
N_REPLICA = 4
N_FSDP = 2


def draw_grad_parts(key, part):
    key_rows, key_cols, key_common, key_private = jax.random.split(key, 4)
    row_scale = jnp.exp(jax.random.uniform(key_rows, (KVW, 1), jnp.float32, math.log(0.5), math.log(2.0)))
    col_scale = jnp.exp(jax.random.uniform(key_cols, (1, D), jnp.float32, math.log(0.5), math.log(2.0)))
    common = jax.random.normal(key_common, (KVW, D), jnp.float32) * row_scale * col_scale
    private = jax.random.normal(key_private, (REPLICAS, N_FSDP, KVW, D), jnp.float32)
    values = jnp.clip(common[None, None] + private, -12.0, 12.0)
    return values.astype(jnp.bfloat16)


def level_of(rng, shape, cuts, low, largest):
    loudness, own = 1.0, jax.random.fold_in(rng, 6)
    for position, shards_of in cuts:
        heights = jnp.exp(jax.random.uniform(jax.random.fold_in(own, position), (shards_of,), jnp.float32, low / len(cuts), largest / len(cuts)))
        loudness = loudness * jnp.repeat(heights, shape[position] // shards_of).reshape([-1 if axis == position else 1 for axis in range(len(shape))])
    return loudness


def scatter_about(stream_key, dims, spread, most, cuts=(), dtype=jnp.bfloat16):
    entries = spread * jax.random.normal(stream_key, dims, jnp.float32)
    if cuts:
        entries = entries * level_of(stream_key, dims, cuts, -0.22, 0.18)
    return jnp.clip(entries, -most, most).astype(dtype)


def setup_inputs(seed: int = 0) -> dict:
    key_of = jax.random.split(jax.random.key(seed), 7)
    grad_parts = draw_grad_parts(jax.random.fold_in(key_of[6], 71), 0)
    inner_params = scatter_about(key_of[1], (REPLICAS, KVW, D), 0.02, 0.12, ((0, 4), (1, 4), (2, 2)), jnp.float32)
    first_moment = scatter_about(key_of[2], (REPLICAS, KVW, D), 0.5, 4.0, ((0, 4), (1, 4), (2, 2)), jnp.float32)
    second_moment = jnp.clip(jnp.exp(math.log(10.0) - 4.6051702 * jax.random.uniform(key_of[3], (REPLICAS, KVW, D), jnp.float32) ** level_of(key_of[3], (REPLICAS, KVW, D), ((0, 4), (1, 4), (2, 2)), -0.2, 0.2)), 0.1, 10.0)
    outer_params = scatter_about(key_of[4], (REPLICAS, KVW, OUTER_COLS), 0.02, 0.12, ((0, 4), (1, 4), (2, 2)), jnp.float32)
    outer_momentum = scatter_about(key_of[5], (REPLICAS, KVW, OUTER_COLS), 0.01, 0.06, ((0, 4), (1, 4), (2, 2)), jnp.float32)
    return dict(grad_parts=grad_parts, inner_params=inner_params, first_moment=first_moment, second_moment=second_moment, outer_params=outer_params, outer_momentum=outer_momentum)


beta_first = 0.9
beta_second = 0.95
inner_rate = 0.01
weight_decay = 0.1
epsilon = 1e-08
outer_rate = 0.7
momentum_factor = 0.9

def inner_adamw(gradient, params, first_in, second_in):
    first_out = beta_first * first_in + (1.0 - beta_first) * gradient
    second_out = beta_second * second_in + (1.0 - beta_second) * gradient * gradient
    first_scale = 1.0 / (1.0 - beta_first ** STEP)
    second_scale = 1.0 / (1.0 - beta_second ** STEP)
    direction = first_out * first_scale / (jnp.sqrt(second_out * second_scale) + epsilon)
    updated = params - inner_rate * (direction + weight_decay * params)
    return (first_out, second_out, updated)

def nesterov(mean_params, outer_in, momentum):
    pseudo_grad = outer_in - mean_params
    momentum_new = momentum_factor * momentum + pseudo_grad
    params_new = outer_in - outer_rate * (pseudo_grad + momentum_factor * momentum_new)
    return (params_new, momentum_new)

def to_full(shares):
    return shares.reshape(N_REPLICA, KVW, N_FSDP, SHARE).transpose(1, 2, 0, 3).reshape(KVW, D)

def to_shares(full):
    return full.reshape(KVW, N_FSDP, N_REPLICA, SHARE).transpose(2, 0, 1, 3).reshape(N_REPLICA, KVW, N_FSDP * SHARE)

def reference(grad_parts, inner_params, first_moment, second_moment, outer_params, outer_momentum):
    gradient = jnp.zeros(inner_params.shape, jnp.float32)
    for index in range(N_FSDP):
        gradient = gradient + grad_parts[:, index].astype(jnp.float32)
    first_out, second_out, updated = inner_adamw(gradient, inner_params, first_moment, second_moment)
    mean_params = lax.optimization_barrier(jnp.sum(updated, axis=0)) / N_REPLICA
    params_new, momentum_new = nesterov(mean_params, to_full(outer_params), to_full(outer_momentum))
    return (params_new, to_shares(params_new), to_shares(momentum_new), first_out, second_out)
```

```python
import jax
import jax.numpy as jnp
from jax import lax
from jax.sharding import PartitionSpec as P

STEP = 100


beta_first = 0.9
beta_second = 0.95
inner_rate = 0.01
weight_decay = 0.1
epsilon = 1e-08
outer_rate = 0.7
momentum_factor = 0.9


def inner_adamw(gradient, params, first_in, second_in):
    first_out = beta_first * first_in + (1.0 - beta_first) * gradient
    second_out = beta_second * second_in + (1.0 - beta_second) * gradient * gradient
    first_scale = 1.0 / (1.0 - beta_first**STEP)
    second_scale = 1.0 / (1.0 - beta_second**STEP)
    direction = first_out * first_scale / (jnp.sqrt(second_out * second_scale) + epsilon)
    updated = params - inner_rate * (direction + weight_decay * params)
    return (first_out, second_out, updated)


def nesterov(mean_params, outer_in, momentum):
    pseudo_grad = outer_in - mean_params
    momentum_new = momentum_factor * momentum + pseudo_grad
    params_new = outer_in - outer_rate * (pseudo_grad + momentum_factor * momentum_new)
    return (params_new, momentum_new)


def shifted(count, step, stride=1, offset=None):
    pairs = []
    for i in range(count):
        group, lane = divmod(i, stride)
        pairs.append((i, ((group + step) % (count // stride)) * stride + lane))
    return pairs


def partner(count):
    return [(i, i ^ 1) for i in range(count)]


def columns(value, index, width):
    return lax.dynamic_slice_in_dim(value, index * width, width, axis=1)


def fsdp_sum(partial):
    fsdp_count = lax.axis_size("fsdp")
    me = lax.axis_index("fsdp")
    cols = partial.shape[1] // fsdp_count
    gradient = columns(partial, me, cols).astype(jnp.float32)
    for step in range(1, fsdp_count):
        send = columns(partial, (me + step) % fsdp_count, cols)
        got = lax.ppermute(send, "fsdp", shifted(fsdp_count, step))
        gradient = gradient + got.astype(jnp.float32)
    return gradient


def replica_sum(updated, share_cols):
    replicas = lax.axis_size("replica")
    pairs = replicas // 2
    me = lax.axis_index("replica")
    core, pair = me % 2, me // 2
    keep = jnp.concatenate([columns(updated, 2 * q + core, share_cols) for q in range(pairs)], axis=1)
    send = jnp.concatenate([columns(updated, 2 * q + 1 - core, share_cols) for q in range(pairs)], axis=1)
    part = keep + lax.ppermute(send, "replica", partner(replicas))
    total = columns(part, pair, share_cols)
    for step in range(1, pairs):
        send = columns(part, (pair + step) % pairs, share_cols)
        total = total + lax.ppermute(send, "replica", shifted(replicas, step, stride=2))
    return total


def gather_weights(share):
    replicas = lax.axis_size("replica")
    fsdp_count = lax.axis_size("fsdp")
    pairs = replicas // 2
    me = lax.axis_index("replica")
    core, pair = me % 2, me // 2
    f_me = lax.axis_index("fsdp")
    row_count, share_cols = share.shape
    out = jnp.zeros((row_count, fsdp_count * replicas * share_cols), share.dtype)

    def put(buf, value, f, q, c):
        return lax.dynamic_update_slice_in_dim(buf, value, ((f * pairs + q) * 2 + c) * share_cols, axis=1)

    out = put(out, share, f_me, pair, core)
    out = put(out, lax.ppermute(share, "replica", partner(replicas)), f_me, pair, 1 - core)
    held = [(share, f_me)]
    for step in range(1, fsdp_count):
        got = lax.ppermute(share, "fsdp", shifted(fsdp_count, step))
        f_src = (f_me + fsdp_count - step) % fsdp_count
        out = put(out, got, f_src, pair, core)
        held.append((got, f_src))
    for got, f_src in held[1:]:
        out = put(out, lax.ppermute(got, "replica", partner(replicas)), f_src, pair, 1 - core)
    stacked = jnp.concatenate([value for value, _ in held], axis=1)
    sources = [f_src for _, f_src in held]
    for step in range(1, pairs):
        got = lax.ppermute(stacked, "replica", shifted(replicas, step, stride=2))
        q_src = (pair + pairs - step) % pairs
        twin = lax.ppermute(got, "replica", partner(replicas))
        for index, f_src in enumerate(sources):
            out = put(out, columns(got, index, share_cols), f_src, q_src, core)
            out = put(out, columns(twin, index, share_cols), f_src, q_src, 1 - core)
    return out


def local(grad_parts, inner_params, first_moment, second_moment, outer_params, outer_momentum):
    replicas = lax.axis_size("replica")
    gradient = fsdp_sum(grad_parts[0, 0])
    first_out, second_out, updated = inner_adamw(
        gradient, inner_params[0], first_moment[0], second_moment[0]
    )
    share_cols = outer_params.shape[2]
    totals = replica_sum(updated, share_cols)
    params_new, momentum_new = nesterov(totals / replicas, outer_params[0], outer_momentum[0])
    next_weights = gather_weights(params_new)
    return (next_weights, params_new[None], momentum_new[None], first_out[None], second_out[None])


def solution(mesh):
    return jax.shard_map(
        local,
        mesh=mesh,
        in_specs=(
            P("replica", "fsdp", "tensor", None),
            P("replica", "tensor", "fsdp"),
            P("replica", "tensor", "fsdp"),
            P("replica", "tensor", "fsdp"),
            P("replica", "tensor", "fsdp"),
            P("replica", "tensor", "fsdp"),
        ),
        out_specs=(
            P("tensor", None),
            P("replica", "tensor", "fsdp"),
            P("replica", "tensor", "fsdp"),
            P("replica", "tensor", "fsdp"),
            P("replica", "tensor", "fsdp"),
        ),
        check_vma=False,
    )
```

```python
import jax
import jax.numpy as jnp
from jax import lax
from jax.sharding import PartitionSpec as P

STEP = 100


beta_first = 0.9
beta_second = 0.95
inner_rate = 0.01
weight_decay = 0.1
epsilon = 1e-08
outer_rate = 0.7
momentum_factor = 0.9


def inner_adamw(gradient, params, first_in, second_in):
    first_out = beta_first * first_in + (1.0 - beta_first) * gradient
    second_out = beta_second * second_in + (1.0 - beta_second) * gradient * gradient
    first_scale = 1.0 / (1.0 - beta_first**STEP)
    second_scale = 1.0 / (1.0 - beta_second**STEP)
    direction = first_out * first_scale / (jnp.sqrt(second_out * second_scale) + epsilon)
    updated = params - inner_rate * (direction + weight_decay * params)
    return (first_out, second_out, updated)


def nesterov(mean_params, outer_in, momentum):
    pseudo_grad = outer_in - mean_params
    momentum_new = momentum_factor * momentum + pseudo_grad
    params_new = outer_in - outer_rate * (pseudo_grad + momentum_factor * momentum_new)
    return (params_new, momentum_new)


def shifted(count, step, stride=1, offset=None):
    pairs = []
    for i in range(count):
        group, lane = divmod(i, stride)
        pairs.append((i, ((group + step) % (count // stride)) * stride + lane))
    return pairs


def partner(count):
    return [(i, i ^ 1) for i in range(count)]


def columns(value, index, width):
    return lax.dynamic_slice_in_dim(value, index * width, width, axis=1)


def fsdp_sum(partial):
    fsdp_count = lax.axis_size("fsdp")
    me = lax.axis_index("fsdp")
    cols = partial.shape[1] // fsdp_count
    gradient = columns(partial, me, cols).astype(jnp.float32)
    for step in range(1, fsdp_count):
        send = columns(partial, (me + step) % fsdp_count, cols)
        got = lax.ppermute(send, "fsdp", shifted(fsdp_count, step))
        gradient = gradient + got.astype(jnp.float32)
    return gradient


def replica_sum(updated, share_cols):
    replicas = lax.axis_size("replica")
    pairs = replicas // 2
    me = lax.axis_index("replica")
    core, pair = me % 2, me // 2
    keep = jnp.concatenate([columns(updated, 2 * q + core, share_cols) for q in range(pairs)], axis=1)
    send = jnp.concatenate([columns(updated, 2 * q + 1 - core, share_cols) for q in range(pairs)], axis=1)
    part = keep + lax.ppermute(send, "replica", partner(replicas))
    total = columns(part, pair, share_cols)
    for step in range(1, pairs):
        send = columns(part, (pair + step) % pairs, share_cols)
        total = total + lax.ppermute(send, "replica", shifted(replicas, step, stride=2))
    return total


def gather_weights(share):
    replicas = lax.axis_size("replica")
    fsdp_count = lax.axis_size("fsdp")
    pairs = replicas // 2
    me = lax.axis_index("replica")
    core, pair = me % 2, me // 2
    f_me = lax.axis_index("fsdp")
    row_count, share_cols = share.shape
    pieces = [(share, f_me, pair, core)]
    pieces.append((lax.ppermute(share, "replica", partner(replicas)), f_me, pair, 1 - core))
    along_x = {}
    for step in range(1, fsdp_count):
        along_x[step] = lax.ppermute(share, "fsdp", shifted(fsdp_count, step))
    along_y = {}
    for step in range(1, pairs):
        along_y[step] = lax.ppermute(share, "replica", shifted(replicas, step, stride=2))
    held = [(value, (f_me + fsdp_count - step) % fsdp_count, pair) for step, value in along_x.items()]
    held += [(value, f_me, (pair + pairs - step) % pairs) for step, value in along_y.items()]
    for step_f in range(1, fsdp_count):
        for step_q in range(1, pairs):
            payload = jnp.where(core == 0, along_y[step_q], along_x[step_f])
            routes = []
            for r in range(replicas):
                for f in range(fsdp_count):
                    q, c = divmod(r, 2)
                    if c == 0:
                        routes.append((r * fsdp_count + f, r * fsdp_count + (f + step_f) % fsdp_count))
                    else:
                        routes.append((r * fsdp_count + f, (((q + step_q) % pairs) * 2 + c) * fsdp_count + f))
            got = lax.ppermute(payload, ("replica", "fsdp"), routes)
            held.append((got, (f_me + fsdp_count - step_f) % fsdp_count, (pair + pairs - step_q) % pairs))
    stacked = jnp.concatenate([value for value, _, _ in held], axis=1)
    twin = lax.ppermute(stacked, "replica", partner(replicas))
    for index, (value, f_src, q_src) in enumerate(held):
        pieces.append((value, f_src, q_src, core))
        pieces.append((columns(twin, index, share_cols), f_src, q_src, 1 - core))
    out = jnp.zeros((row_count, fsdp_count * replicas * share_cols), share.dtype)
    for value, f, q, c in pieces:
        out = lax.dynamic_update_slice_in_dim(out, value, ((f * pairs + q) * 2 + c) * share_cols, axis=1)
    return out


CHUNKS = 4


def local(grad_parts, inner_params, first_moment, second_moment, outer_params, outer_momentum):
    replicas = lax.axis_size("replica")
    share_cols = outer_params.shape[2]
    row_count = inner_params.shape[1]
    chunk = row_count // CHUNKS
    pieces = []
    for index in range(CHUNKS):
        rows = slice(index * chunk, (index + 1) * chunk)
        gradient = fsdp_sum(grad_parts[0, 0, rows])
        first_out, second_out, updated = inner_adamw(
            gradient, inner_params[0, rows], first_moment[0, rows], second_moment[0, rows]
        )
        totals = replica_sum(updated, share_cols)
        params_new, momentum_new = nesterov(totals / replicas, outer_params[0, rows], outer_momentum[0, rows])
        next_weights = gather_weights(params_new)
        pieces.append((next_weights, params_new, momentum_new, first_out, second_out))
    outs = [jnp.concatenate(parts, axis=0) for parts in zip(*pieces)]
    next_weights, params_new, momentum_new, first_out, second_out = outs
    return (next_weights, params_new[None], momentum_new[None], first_out[None], second_out[None])


def solution(mesh):
    return jax.shard_map(
        local,
        mesh=mesh,
        in_specs=(
            P("replica", "fsdp", "tensor", None),
            P("replica", "tensor", "fsdp"),
            P("replica", "tensor", "fsdp"),
            P("replica", "tensor", "fsdp"),
            P("replica", "tensor", "fsdp"),
            P("replica", "tensor", "fsdp"),
        ),
        out_specs=(
            P("tensor", None),
            P("replica", "tensor", "fsdp"),
            P("replica", "tensor", "fsdp"),
            P("replica", "tensor", "fsdp"),
            P("replica", "tensor", "fsdp"),
        ),
        check_vma=False,
    )
```

```python
import jax
import jax.numpy as jnp
from jax import lax
from jax.sharding import PartitionSpec as P

STEP = 100


beta_first = 0.9
beta_second = 0.95
inner_rate = 0.01
weight_decay = 0.1
epsilon = 1e-08
outer_rate = 0.7
momentum_factor = 0.9


def inner_adamw(gradient, params, first_in, second_in):
    first_out = beta_first * first_in + (1.0 - beta_first) * gradient
    second_out = beta_second * second_in + (1.0 - beta_second) * gradient * gradient
    first_scale = 1.0 / (1.0 - beta_first**STEP)
    second_scale = 1.0 / (1.0 - beta_second**STEP)
    direction = first_out * first_scale / (jnp.sqrt(second_out * second_scale) + epsilon)
    updated = params - inner_rate * (direction + weight_decay * params)
    return (first_out, second_out, updated)


def nesterov(mean_params, outer_in, momentum):
    pseudo_grad = outer_in - mean_params
    momentum_new = momentum_factor * momentum + pseudo_grad
    params_new = outer_in - outer_rate * (pseudo_grad + momentum_factor * momentum_new)
    return (params_new, momentum_new)


def shifted(count, step, stride=1, offset=None):
    pairs = []
    for i in range(count):
        group, lane = divmod(i, stride)
        pairs.append((i, ((group + step) % (count // stride)) * stride + lane))
    return pairs


def partner(count):
    return [(i, i ^ 1) for i in range(count)]


def columns(value, index, width):
    return lax.dynamic_slice_in_dim(value, index * width, width, axis=1)


def fsdp_sum(partial):
    fsdp_count = lax.axis_size("fsdp")
    me = lax.axis_index("fsdp")
    cols = partial.shape[1] // fsdp_count
    gradient = columns(partial, me, cols).astype(jnp.float32)
    for step in range(1, fsdp_count):
        send = columns(partial, (me + step) % fsdp_count, cols)
        got = lax.ppermute(send, "fsdp", shifted(fsdp_count, step))
        gradient = gradient + got.astype(jnp.float32)
    return gradient


def replica_sum(updated, share_cols):
    replicas = lax.axis_size("replica")
    pairs = replicas // 2
    me = lax.axis_index("replica")
    core, pair = me % 2, me // 2
    keep = jnp.concatenate([columns(updated, 2 * q + core, share_cols) for q in range(pairs)], axis=1)
    send = jnp.concatenate([columns(updated, 2 * q + 1 - core, share_cols) for q in range(pairs)], axis=1)
    part = keep + lax.ppermute(send, "replica", partner(replicas))
    total = columns(part, pair, share_cols)
    for step in range(1, pairs):
        send = columns(part, (pair + step) % pairs, share_cols)
        total = total + lax.ppermute(send, "replica", shifted(replicas, step, stride=2))
    return total


def gather_weights(share):
    replicas = lax.axis_size("replica")
    fsdp_count = lax.axis_size("fsdp")
    pairs = replicas // 2
    me = lax.axis_index("replica")
    core, pair = me % 2, me // 2
    f_me = lax.axis_index("fsdp")
    row_count, share_cols = share.shape
    pieces = [(share, f_me, pair, core)]
    pieces.append((lax.ppermute(share, "replica", partner(replicas)), f_me, pair, 1 - core))
    along_x = {}
    for step in range(1, fsdp_count):
        along_x[step] = lax.ppermute(share, "fsdp", shifted(fsdp_count, step))
    along_y = {}
    for step in range(1, pairs):
        along_y[step] = lax.ppermute(share, "replica", shifted(replicas, step, stride=2))
    held = [(value, (f_me + fsdp_count - step) % fsdp_count, pair) for step, value in along_x.items()]
    held += [(value, f_me, (pair + pairs - step) % pairs) for step, value in along_y.items()]
    for step_f in range(1, fsdp_count):
        for step_q in range(1, pairs):
            payload = jnp.where(core == 0, along_y[step_q], along_x[step_f])
            routes = []
            for r in range(replicas):
                for f in range(fsdp_count):
                    q, c = divmod(r, 2)
                    if c == 0:
                        routes.append((r * fsdp_count + f, r * fsdp_count + (f + step_f) % fsdp_count))
                    else:
                        routes.append((r * fsdp_count + f, (((q + step_q) % pairs) * 2 + c) * fsdp_count + f))
            got = lax.ppermute(payload, ("replica", "fsdp"), routes)
            held.append((got, (f_me + fsdp_count - step_f) % fsdp_count, (pair + pairs - step_q) % pairs))
    stacked = jnp.concatenate([value for value, _, _ in held], axis=1)
    twin = lax.ppermute(stacked, "replica", partner(replicas))
    for index, (value, f_src, q_src) in enumerate(held):
        pieces.append((value, f_src, q_src, core))
        pieces.append((columns(twin, index, share_cols), f_src, q_src, 1 - core))
    out = jnp.zeros((row_count, fsdp_count * replicas * share_cols), share.dtype)
    for value, f, q, c in pieces:
        out = lax.dynamic_update_slice_in_dim(out, value, ((f * pairs + q) * 2 + c) * share_cols, axis=1)
    return out


CHUNK_WEIGHTS = (2, 4, 5, 5)


def chunk_rows(row_count):
    unit = row_count // sum(CHUNK_WEIGHTS)
    if unit % 8 or unit * sum(CHUNK_WEIGHTS) != row_count:
        return [row_count // 4] * 4
    return [unit * w for w in CHUNK_WEIGHTS]


def local(grad_parts, inner_params, first_moment, second_moment, outer_params, outer_momentum):
    replicas = lax.axis_size("replica")
    share_cols = outer_params.shape[2]
    pieces = []
    begin = 0
    for size in chunk_rows(inner_params.shape[1]):
        rows = slice(begin, begin + size)
        begin += size
        gradient = fsdp_sum(grad_parts[0, 0, rows])
        first_out, second_out, updated = inner_adamw(
            gradient, inner_params[0, rows], first_moment[0, rows], second_moment[0, rows]
        )
        totals = replica_sum(updated, share_cols)
        params_new, momentum_new = nesterov(totals / replicas, outer_params[0, rows], outer_momentum[0, rows])
        next_weights = gather_weights(params_new)
        pieces.append((next_weights, params_new, momentum_new, first_out, second_out))
    outs = [jnp.concatenate(parts, axis=0) for parts in zip(*pieces)]
    next_weights, params_new, momentum_new, first_out, second_out = outs
    return (next_weights, params_new[None], momentum_new[None], first_out[None], second_out[None])


def solution(mesh):
    return jax.shard_map(
        local,
        mesh=mesh,
        in_specs=(
            P("replica", "fsdp", "tensor", None),
            P("replica", "tensor", "fsdp"),
            P("replica", "tensor", "fsdp"),
            P("replica", "tensor", "fsdp"),
            P("replica", "tensor", "fsdp"),
            P("replica", "tensor", "fsdp"),
        ),
        out_specs=(
            P("tensor", None),
            P("replica", "tensor", "fsdp"),
            P("replica", "tensor", "fsdp"),
            P("replica", "tensor", "fsdp"),
            P("replica", "tensor", "fsdp"),
        ),
        check_vma=False,
    )
```

```python
import jax
import jax.numpy as jnp
from jax import lax
from jax.sharding import PartitionSpec as P

STEP = 100


beta_first = 0.9
beta_second = 0.95
inner_rate = 0.01
weight_decay = 0.1
epsilon = 1e-08
outer_rate = 0.7
momentum_factor = 0.9


def inner_adamw(gradient, params, first_in, second_in):
    first_out = beta_first * first_in + (1.0 - beta_first) * gradient
    second_out = beta_second * second_in + (1.0 - beta_second) * gradient * gradient
    first_scale = 1.0 / (1.0 - beta_first**STEP)
    second_scale = 1.0 / (1.0 - beta_second**STEP)
    direction = first_out * first_scale / (jnp.sqrt(second_out * second_scale) + epsilon)
    updated = params - inner_rate * (direction + weight_decay * params)
    return (first_out, second_out, updated)


def nesterov(mean_params, outer_in, momentum):
    pseudo_grad = outer_in - mean_params
    momentum_new = momentum_factor * momentum + pseudo_grad
    params_new = outer_in - outer_rate * (pseudo_grad + momentum_factor * momentum_new)
    return (params_new, momentum_new)


def shifted(count, step, stride=1, offset=None):
    pairs = []
    for i in range(count):
        group, lane = divmod(i, stride)
        pairs.append((i, ((group + step) % (count // stride)) * stride + lane))
    return pairs


def partner(count):
    return [(i, i ^ 1) for i in range(count)]


def columns(value, index, width):
    return lax.dynamic_slice_in_dim(value, index * width, width, axis=1)


def fsdp_sum(partial):
    fsdp_count = lax.axis_size("fsdp")
    me = lax.axis_index("fsdp")
    cols = partial.shape[1] // fsdp_count
    gradient = columns(partial, me, cols).astype(jnp.float32)
    for step in range(1, fsdp_count):
        send = columns(partial, (me + step) % fsdp_count, cols)
        got = lax.ppermute(send, "fsdp", shifted(fsdp_count, step))
        gradient = gradient + got.astype(jnp.float32)
    return gradient


def replica_sum(updated, share_cols):
    replicas = lax.axis_size("replica")
    pairs = replicas // 2
    me = lax.axis_index("replica")
    core, pair = me % 2, me // 2
    keep = jnp.concatenate([columns(updated, 2 * q + core, share_cols) for q in range(pairs)], axis=1)
    send = jnp.concatenate([columns(updated, 2 * q + 1 - core, share_cols) for q in range(pairs)], axis=1)
    part = keep + lax.ppermute(send, "replica", partner(replicas))
    total = columns(part, pair, share_cols)
    for step in range(1, pairs):
        send = columns(part, (pair + step) % pairs, share_cols)
        total = total + lax.ppermute(send, "replica", shifted(replicas, step, stride=2))
    return total


def gather_weights(share):
    replicas = lax.axis_size("replica")
    fsdp_count = lax.axis_size("fsdp")
    pairs = replicas // 2
    me = lax.axis_index("replica")
    core, pair = me % 2, me // 2
    f_me = lax.axis_index("fsdp")
    row_count, share_cols = share.shape
    pieces = []
    along_x = {}
    for step in range(1, fsdp_count):
        along_x[step] = lax.ppermute(share, "fsdp", shifted(fsdp_count, step))
    along_y = {}
    for step in range(1, pairs):
        along_y[step] = lax.ppermute(share, "replica", shifted(replicas, step, stride=2))
    held = [(value, (f_me + fsdp_count - step) % fsdp_count, pair) for step, value in along_x.items()]
    held += [(value, f_me, (pair + pairs - step) % pairs) for step, value in along_y.items()]
    for step_f in range(1, fsdp_count):
        for step_q in range(1, pairs):
            payload = jnp.where(core == 0, along_y[step_q], along_x[step_f])
            routes = []
            for r in range(replicas):
                for f in range(fsdp_count):
                    q, c = divmod(r, 2)
                    if c == 0:
                        routes.append((r * fsdp_count + f, r * fsdp_count + (f + step_f) % fsdp_count))
                    else:
                        routes.append((r * fsdp_count + f, (((q + step_q) % pairs) * 2 + c) * fsdp_count + f))
            got = lax.ppermute(payload, ("replica", "fsdp"), routes)
            held.append((got, (f_me + fsdp_count - step_f) % fsdp_count, (pair + pairs - step_q) % pairs))
    held.append((share, f_me, pair))
    stacked = jnp.concatenate([value for value, _, _ in held], axis=1)
    twin = lax.ppermute(stacked, "replica", partner(replicas))
    for index, (value, f_src, q_src) in enumerate(held):
        pieces.append((value, f_src, q_src, core))
        pieces.append((columns(twin, index, share_cols), f_src, q_src, 1 - core))
    out = jnp.zeros((row_count, fsdp_count * replicas * share_cols), share.dtype)
    for value, f, q, c in pieces:
        out = lax.dynamic_update_slice_in_dim(out, value, ((f * pairs + q) * 2 + c) * share_cols, axis=1)
    return out


CHUNK_WEIGHTS = (2, 4, 5, 5)


def chunk_rows(row_count):
    unit = row_count // sum(CHUNK_WEIGHTS)
    if unit % 8 or unit * sum(CHUNK_WEIGHTS) != row_count:
        return [row_count // 4] * 4
    return [unit * w for w in CHUNK_WEIGHTS]


def local(grad_parts, inner_params, first_moment, second_moment, outer_params, outer_momentum):
    replicas = lax.axis_size("replica")
    share_cols = outer_params.shape[2]
    pieces = []
    begin = 0
    for size in chunk_rows(inner_params.shape[1]):
        rows = slice(begin, begin + size)
        begin += size
        gradient = fsdp_sum(grad_parts[0, 0, rows])
        first_out, second_out, updated = inner_adamw(
            gradient, inner_params[0, rows], first_moment[0, rows], second_moment[0, rows]
        )
        totals = replica_sum(updated, share_cols)
        params_new, momentum_new = nesterov(totals / replicas, outer_params[0, rows], outer_momentum[0, rows])
        next_weights = gather_weights(params_new)
        pieces.append((next_weights, params_new, momentum_new, first_out, second_out))
    outs = [jnp.concatenate(parts, axis=0) for parts in zip(*pieces)]
    next_weights, params_new, momentum_new, first_out, second_out = outs
    return (next_weights, params_new[None], momentum_new[None], first_out[None], second_out[None])


def solution(mesh):
    return jax.shard_map(
        local,
        mesh=mesh,
        in_specs=(
            P("replica", "fsdp", "tensor", None),
            P("replica", "tensor", "fsdp"),
            P("replica", "tensor", "fsdp"),
            P("replica", "tensor", "fsdp"),
            P("replica", "tensor", "fsdp"),
            P("replica", "tensor", "fsdp"),
        ),
        out_specs=(
            P("tensor", None),
            P("replica", "tensor", "fsdp"),
            P("replica", "tensor", "fsdp"),
            P("replica", "tensor", "fsdp"),
            P("replica", "tensor", "fsdp"),
        ),
        check_vma=False,
    )
```
